256 devices in a mesh: blk: 8 (over y, x_hi), grp: 32 (over x_lo, z, core).
Axes of the slice: x: 4 (x_hi: 2, x_lo: 2; x = x_hi * 2 + x_lo), y: 4, z: 8, core: 2. Of those that a mesh axis runs over, the one named last changes fastest.
Arguments:
- position: float32 [3, 65536], P(None, ('blk', 'grp'))
- velocity: float32 [3, 65536], P(None, ('blk', 'grp')), may hold values from -3 to 3
- accel_old: float32 [3, 65536], P(None, ('blk', 'grp')), may hold values from -5 to 5
- jerk_old: float32 [3, 65536], P(None, ('blk', 'grp')), may hold values from -5 to 5
- elapsed: float32 [65536], P(('blk', 'grp')), may hold values from 0.01 to 0.1
- masses: float32 [65536], P(('blk', 'grp'))
- active_stars: int32 [8192], P(('blk', 'grp')), may hold values from 0 to 255, as said below
- neighbour_list: int32 [256, 64], P(('blk', 'grp')), may hold values from 0 to 63, as said below
- neighbour_count: int32 [256], P(('blk', 'grp')), may hold values from 1 to 64, as said below
Outputs:
- regular: float32 [6, 8192], P(None, ('blk', 'grp'))
- irregular: float32 [6, 8192], P(None, ('blk', 'grp'))
- correction: float32 [6, 8192], P(None, ('blk', 'grp'))
The draws below stay inside these ranges and needn't reach their ends.
Inputs may be any that keep to these rules, and one draw needn't show every extreme that they name: `active_stars`: the 32 entries of one device are distinct local indices of that device's stars, all inside one block of 128 of them. `neighbour_list`: row r lists neighbour blocks for the active stars of device r, numbered within r's group (2 blocks a device, devices in grp order). Its first neighbour_count[r] entries are distinct and ascending, at most 2 of them from one device, and include the block that holds r's active stars; later entries mean nothing. `neighbour_count`: in every group along blk some device lists 2 blocks of every device of its group.
All inputs are finite; a program needn't handle non-finite values.
Results may differ from the reference program's by a relative error of at most 0.0003.
Values sent between devices are 32-bit elements; how exact they have to be, the bound alone decides.
No kernel may reach another device: no remote copies, remote signals or barrier semaphores. Data moves between devices by JAX's collectives and lax.ppermute only.
A program may use at most 64 MiB of HBM per device.

```python
import math
import jax
import jax.numpy as jnp
from jax import lax

RES_DEV = 256
ACT_DEV = 32
BLOCK = 128
NBL = 64
NSTARS = 65536
ACTIVE = 8192
N_BLK = 8
N_GRP = 32


def draw_position(key, part):
    spots = jax.random.uniform(jax.random.fold_in(key, 11), (3, NSTARS), jnp.float32, -1.0, 1.0)
    return spots


def draw_masses(key, part):
    levels = jax.random.uniform(jax.random.fold_in(key, 23), (NSTARS,), jnp.float32, jnp.log(0.3), jnp.log(3.0))
    return jnp.exp(levels) / NSTARS


def list_tables(key):
    owners = N_BLK * N_GRP
    blk_dev = RES_DEV // BLOCK
    keys = jax.random.split(jax.random.fold_in(key, 7001), 8)
    home = jax.random.randint(keys[0], (owners,), 0, blk_dev)
    load = jax.random.randint(keys[1], (owners, 1), 1, 4)
    rolled = jax.random.randint(keys[2], (owners, N_GRP), 0, 4)
    taken = jnp.minimum(2, rolled * load // 3)
    my_slot = jnp.arange(owners) % N_GRP
    holders = jnp.arange(N_GRP)
    is_self = holders[None, :] == my_slot[:, None]
    taken = jnp.where(is_self, jnp.maximum(taken, 1), taken)
    full_owner = jax.random.randint(keys[3], (N_BLK,), 0, N_GRP)
    is_full = my_slot == full_owner[jnp.arange(owners) // N_GRP]
    taken = jnp.where(is_full[:, None], 2, taken)
    first = jax.random.randint(keys[4], (owners, N_GRP), 0, blk_dev)
    first = jnp.where(is_self, home[:, None], first)
    second = (first + 1 + jax.random.randint(keys[5], (owners, N_GRP), 0, blk_dev - 1)) % blk_dev
    slot_low = jnp.where(taken == 2, jnp.minimum(first, second), first)
    slot_high = jnp.maximum(first, second)
    block_ids = jnp.stack([slot_low, slot_high], axis=-1) + holders[None, :, None] * blk_dev
    used = jnp.arange(2)[None, None, :] < taken[:, :, None]
    block_ids = block_ids.reshape(owners, NBL)
    used = used.reshape(owners, NBL)
    place = jnp.cumsum(used.astype(jnp.int32), axis=1) - 1
    target = jnp.where(used, place, NBL)
    filler = jax.random.randint(keys[6], (owners, NBL + 1), 0, N_GRP * blk_dev)
    rows = jnp.arange(owners)[:, None]
    listed = filler.at[rows, target].set(block_ids)[:, :NBL]
    counts = jnp.sum(taken, axis=1).astype(jnp.int32)
    row_keys = jax.random.split(keys[7], owners)
    chosen = jax.vmap(lambda single: jax.random.permutation(single, BLOCK)[:ACT_DEV])(row_keys)
    active = (home[:, None] * BLOCK + chosen).reshape(ACTIVE).astype(jnp.int32)
    return (active, listed.astype(jnp.int32), counts)


def draw_active_stars(key, part):
    return list_tables(key)[0]


def draw_neighbour_list(key, part):
    return list_tables(key)[1]


def draw_neighbour_count(key, part):
    return list_tables(key)[2]


def level_of(key, extent, shards, least, high):
    level, own = 1.0, jax.random.fold_in(key, 6)
    for dim, parts in shards:
        steps = jnp.exp(jax.random.uniform(jax.random.fold_in(own, dim), (parts,), jnp.float32, least / len(shards), high / len(shards)))
        level = level * jnp.repeat(steps, extent[dim] // parts).reshape([-1 if axis == dim else 1 for axis in range(len(extent))])
    return level


def bell_draw(rng, extent, scale, reach, pieces=(), kind=jnp.bfloat16):
    factor_of = level_of(rng, extent, pieces, -0.22, 0.18) if pieces else 1.0
    values = jax.random.normal(rng, extent, jnp.float32) * scale * factor_of
    return jnp.minimum(jnp.maximum(values, -reach), reach).astype(kind)


def setup_inputs(seed: int = 0) -> dict:
    arg_keys = jax.random.split(jax.random.key(seed), 10)
    position = draw_position(jax.random.fold_in(arg_keys[9], 71), 0)
    velocity = bell_draw(arg_keys[1], (3, NSTARS), 0.5, 3.0, ((1, 256),), jnp.float32)
    accel_old = bell_draw(arg_keys[2], (3, NSTARS), 1.0, 5.0, ((1, 256),), jnp.float32)
    jerk_old = bell_draw(arg_keys[3], (3, NSTARS), 1.0, 5.0, ((1, 256),), jnp.float32)
    elapsed = jnp.clip(jnp.exp(math.log(0.1) - 2.3025851 * jax.random.uniform(arg_keys[4], (NSTARS,), jnp.float32) ** level_of(arg_keys[4], (NSTARS,), ((0, 256),), -0.2, 0.2)), 0.01, 0.1)
    masses = draw_masses(jax.random.fold_in(arg_keys[9], 71), 0)
    active_stars = draw_active_stars(jax.random.fold_in(arg_keys[9], 71), 0)
    neighbour_list = draw_neighbour_list(jax.random.fold_in(arg_keys[9], 71), 0)
    neighbour_count = draw_neighbour_count(jax.random.fold_in(arg_keys[9], 71), 0)
    return {"position": position, "velocity": velocity, "accel_old": accel_old, "jerk_old": jerk_old, "elapsed": elapsed, "masses": masses, "active_stars": active_stars, "neighbour_list": neighbour_list, "neighbour_count": neighbour_count}


soften_sq = 0.0001

def two_sums(targets, sources, far_weight, near_weight):
    gap_x = sources[0][None, :] - targets[0][:, None]
    gap_y = sources[1][None, :] - targets[1][:, None]
    gap_z = sources[2][None, :] - targets[2][:, None]
    rel_x = sources[3][None, :] - targets[3][:, None]
    rel_y = sources[4][None, :] - targets[4][:, None]
    rel_z = sources[5][None, :] - targets[5][:, None]
    dist_sq = gap_x * gap_x + gap_y * gap_y + gap_z * gap_z + soften_sq
    inverse = lax.rsqrt(dist_sq)
    inv_cube = inverse * inverse * inverse
    radial = 3.0 * (gap_x * rel_x + gap_y * rel_y + gap_z * rel_z) / dist_sq
    term_list = [gap_x, gap_y, gap_z, rel_x - radial * gap_x, rel_y - radial * gap_y, rel_z - radial * gap_z]
    far_scaled = far_weight * inv_cube
    near_scaled = near_weight * inv_cube
    far_part = jnp.stack([lax.optimization_barrier(jnp.sum(far_scaled * term, axis=1)) for term in term_list])
    near_part = jnp.stack([lax.optimization_barrier(jnp.sum(near_scaled * term, axis=1)) for term in term_list])
    return (far_part, near_part)

def reference(position, velocity, accel_old, jerk_old, elapsed, masses, active_stars, neighbour_list, neighbour_count):
    moved_pos = position + elapsed * (velocity + elapsed * (0.5 * accel_old + elapsed * jerk_old / 6.0))
    turned = velocity + elapsed * (accel_old + 0.5 * elapsed * jerk_old)
    owners = N_BLK * N_GRP
    blk_dev = RES_DEV // BLOCK
    group_blocks = blk_dev * N_GRP
    block_count = NSTARS // BLOCK
    owner_of = jnp.arange(ACTIVE, dtype=jnp.int32) // ACT_DEV
    global_rows = active_stars + owner_of * RES_DEV
    targets = jnp.concatenate([moved_pos[:, global_rows], turned[:, global_rows]], axis=0)
    in_list = jnp.arange(NBL, dtype=jnp.int32)[None, :] < neighbour_count[:, None]
    slot_ids = jnp.where(in_list, neighbour_list, group_blocks)
    owner_rows = jnp.arange(owners, dtype=jnp.int32)[:, None]
    local_member = jnp.zeros((owners, group_blocks + 1), jnp.float32).at[owner_rows, slot_ids].set(1.0)[:, :group_blocks]
    block_ids = jnp.arange(block_count, dtype=jnp.int32)
    same_group = (block_ids // group_blocks)[None, :] == (jnp.arange(owners, dtype=jnp.int32) // N_GRP)[:, None]
    member = jnp.where(same_group, local_member[:, block_ids % group_blocks], 0.0)
    per_batch = 8
    batch_count = owners // per_batch
    piece_size = RES_DEV * 8
    piece_count = NSTARS // piece_size
    target_batches = targets.reshape(6, batch_count, per_batch * ACT_DEV).transpose(1, 0, 2)
    member_batches = member.reshape(batch_count, per_batch, block_count)
    source_all = jnp.concatenate([moved_pos, turned], axis=0).reshape(6, piece_count, piece_size).transpose(1, 0, 2)
    mass_pieces = masses.reshape(piece_count, piece_size)
    piece_index = jnp.arange(piece_count, dtype=jnp.int32)

    def one_batch(items):
        target_block, member_block = items
        row_member = jnp.repeat(member_block, ACT_DEV, axis=0)

        def add_piece(carry, inputs):
            source_block, mass_block, index_now = inputs
            near_blocks = lax.dynamic_slice_in_dim(row_member, index_now * (piece_size // BLOCK), piece_size // BLOCK, 1)
            near_mask = jnp.repeat(near_blocks, BLOCK, axis=1)
            far_part, near_part = two_sums(target_block, source_block, mass_block[None, :] * (1.0 - near_mask), mass_block[None, :] * near_mask)
            return ((carry[0] + far_part, carry[1] + near_part), None)
        zero_sums = jnp.zeros((6, per_batch * ACT_DEV), jnp.float32)
        totals, unused = lax.scan(add_piece, (zero_sums, zero_sums), (source_all, mass_pieces, piece_index))
        return totals
    far_all, near_all = lax.map(one_batch, (target_batches, member_batches))
    regular = far_all.transpose(1, 0, 2).reshape(6, ACTIVE)
    irregular = near_all.transpose(1, 0, 2).reshape(6, ACTIVE)
    accel_now = regular[:3] + irregular[:3]
    jerk_now = regular[3:] + irregular[3:]
    step_time = elapsed[global_rows]
    change = accel_old[:, global_rows] - accel_now
    snap_term = -6.0 * change - step_time * (4.0 * jerk_old[:, global_rows] + 2.0 * jerk_now)
    crackle_term = 12.0 * change + 6.0 * step_time * (jerk_old[:, global_rows] + jerk_now)
    return (regular, irregular, jnp.concatenate([snap_term, crackle_term], axis=0))
```

```python
import jax
import jax.numpy as jnp
from jax import lax
from jax.sharding import PartitionSpec as P

BLOCK = 128


soften_sq = 0.0001


def pair_sums(targets, sources, weight):
    gap_x = sources[0][None, :] - targets[0][:, None]
    gap_y = sources[1][None, :] - targets[1][:, None]
    gap_z = sources[2][None, :] - targets[2][:, None]
    rel_x = sources[3][None, :] - targets[3][:, None]
    rel_y = sources[4][None, :] - targets[4][:, None]
    rel_z = sources[5][None, :] - targets[5][:, None]
    dist_sq = gap_x * gap_x + gap_y * gap_y + gap_z * gap_z + soften_sq
    inverse = lax.rsqrt(dist_sq)
    scaled = weight * (inverse * inverse * inverse)
    radial = 3.0 * (gap_x * rel_x + gap_y * rel_y + gap_z * rel_z) / dist_sq
    term_list = [
        gap_x,
        gap_y,
        gap_z,
        rel_x - radial * gap_x,
        rel_y - radial * gap_y,
        rel_z - radial * gap_z,
    ]
    return jnp.stack([jnp.sum(scaled * term, axis=1) for term in term_list])


def per_device(
    position,
    velocity,
    accel_old,
    jerk_old,
    elapsed,
    masses,
    active_stars,
    neighbour_list,
    neighbour_count,
):
    moved_pos = position + elapsed * (
        velocity + elapsed * (0.5 * accel_old + elapsed * jerk_old / 6.0)
    )
    turned = velocity + elapsed * (accel_old + 0.5 * elapsed * jerk_old)
    sources = jnp.concatenate([moved_pos, turned], axis=0)
    own_set = jnp.take(sources, active_stars, axis=1)
    act_dev = active_stars.shape[0]
    block_data = jnp.concatenate([sources, masses[None, :]], axis=0)
    group = lax.all_gather(block_data, "grp", axis=1, tiled=True)
    group_src = group[:6]
    group_mass = group[6]
    targets = lax.all_gather(own_set, "blk", axis=1, tiled=True)
    blk_size = lax.axis_size("blk")
    blk_here = lax.axis_index("blk")
    block_total = group_src.shape[1] // BLOCK
    slot_total = neighbour_list.shape[1]
    own_live = jnp.arange(slot_total) < neighbour_count[0]
    near = jnp.any(
        own_live[:, None]
        & (neighbour_list[0][:, None] == jnp.arange(block_total)[None, :]),
        axis=0,
    ).astype(jnp.float32)
    owner_rows = jnp.arange(blk_size)
    keep = jnp.where((owner_rows == blk_here)[:, None], 1.0 - near[None, :], 1.0)
    target_pieces = targets.reshape(6, blk_size, act_dev).transpose(1, 0, 2)

    def one_piece(items):
        target_piece, keep_piece = items
        weight = jnp.repeat(keep_piece, BLOCK)[None, :] * group_mass[None, :]
        return pair_sums(target_piece, group_src, weight)

    sums = lax.map(one_piece, (target_pieces, keep))
    partial_terms = sums.transpose(1, 0, 2).reshape(6, blk_size * act_dev)
    regular = lax.psum_scatter(partial_terms, "blk", scatter_dimension=1, tiled=True)
    near_mass = (jnp.repeat(near, BLOCK) * group_mass)[None, :]
    irregular = pair_sums(own_set, group_src, near_mass)
    accel_now = regular[:3] + irregular[:3]
    jerk_now = regular[3:] + irregular[3:]
    step_time = jnp.take(elapsed, active_stars)
    start_accel = jnp.take(accel_old, active_stars, axis=1)
    start_jerk = jnp.take(jerk_old, active_stars, axis=1)
    change = start_accel - accel_now
    snap_term = -6.0 * change - step_time * (4.0 * start_jerk + 2.0 * jerk_now)
    crackle_term = 12.0 * change + 6.0 * step_time * (start_jerk + jerk_now)
    return (regular, irregular, jnp.concatenate([snap_term, crackle_term], axis=0))


def solution(mesh):
    in_specs = (
        P(None, ("blk", "grp")),
        P(None, ("blk", "grp")),
        P(None, ("blk", "grp")),
        P(None, ("blk", "grp")),
        P(("blk", "grp")),
        P(("blk", "grp")),
        P(("blk", "grp")),
        P(("blk", "grp"), None),
        P(("blk", "grp")),
    )
    out_specs = (P(None, ("blk", "grp")), P(None, ("blk", "grp")), P(None, ("blk", "grp")))
    return jax.shard_map(
        per_device, mesh=mesh, in_specs=in_specs, out_specs=out_specs, check_vma=False
    )
```

```python
import jax
import jax.numpy as jnp
from jax import lax
from jax.sharding import PartitionSpec as P

BLOCK = 128


soften_sq = 0.0001


def exchange(block, axis, bit):
    size = lax.axis_size(axis)
    return lax.ppermute(block, axis, [(i, i ^ bit) for i in range(size)])


def gather_doubling(block, axis):
    me = lax.axis_index(axis)
    bit = 1
    while bit < lax.axis_size(axis):
        got = exchange(block, axis, bit)
        upper = (me // bit) % 2 == 1
        block = jnp.where(
            upper, jnp.concatenate([got, block], 1), jnp.concatenate([block, got], 1)
        )
        bit *= 2
    return block


def reduce_halving(block, axis):
    me = lax.axis_index(axis)
    bit = lax.axis_size(axis) // 2
    while bit >= 1:
        width = block.shape[1] // 2
        low, high = block[:, :width], block[:, width:]
        upper = (me // bit) % 2 == 1
        keep = jnp.where(upper, high, low)
        send = jnp.where(upper, low, high)
        block = keep + exchange(send, axis, bit)
        bit //= 2
    return block


def gather_all_to_all(block, axis):
    size = lax.axis_size(axis)
    spread = jnp.broadcast_to(block[:, None, :], (block.shape[0], size, block.shape[1]))
    got = lax.all_to_all(spread, axis, 1, 1, tiled=True)
    return got.reshape(block.shape[0], size * block.shape[1])


def pair_sums(targets, sources, weight):
    gap_x = sources[0][None, :] - targets[0][:, None]
    gap_y = sources[1][None, :] - targets[1][:, None]
    gap_z = sources[2][None, :] - targets[2][:, None]
    rel_x = sources[3][None, :] - targets[3][:, None]
    rel_y = sources[4][None, :] - targets[4][:, None]
    rel_z = sources[5][None, :] - targets[5][:, None]
    dist_sq = gap_x * gap_x + gap_y * gap_y + gap_z * gap_z + soften_sq
    inverse = lax.rsqrt(dist_sq)
    scaled = weight * (inverse * inverse * inverse)
    radial = 3.0 * (gap_x * rel_x + gap_y * rel_y + gap_z * rel_z) / dist_sq
    term_list = [
        gap_x,
        gap_y,
        gap_z,
        rel_x - radial * gap_x,
        rel_y - radial * gap_y,
        rel_z - radial * gap_z,
    ]
    return jnp.stack([jnp.sum(scaled * term, axis=1) for term in term_list])


def per_device(
    position,
    velocity,
    accel_old,
    jerk_old,
    elapsed,
    masses,
    active_stars,
    neighbour_list,
    neighbour_count,
):
    moved_pos = position + elapsed * (
        velocity + elapsed * (0.5 * accel_old + elapsed * jerk_old / 6.0)
    )
    turned = velocity + elapsed * (accel_old + 0.5 * elapsed * jerk_old)
    sources = jnp.concatenate([moved_pos, turned], axis=0)
    own_set = jnp.take(sources, active_stars, axis=1)
    act_dev = active_stars.shape[0]
    block_data = jnp.concatenate([sources, masses[None, :]], axis=0)
    group = gather_all_to_all(block_data, "grp")
    group_src = group[:6]
    group_mass = group[6]
    targets = gather_doubling(own_set, "blk")
    blk_size = lax.axis_size("blk")
    blk_here = lax.axis_index("blk")
    block_total = group_src.shape[1] // BLOCK
    slot_total = neighbour_list.shape[1]
    own_live = jnp.arange(slot_total) < neighbour_count[0]
    near = jnp.any(
        own_live[:, None]
        & (neighbour_list[0][:, None] == jnp.arange(block_total)[None, :]),
        axis=0,
    ).astype(jnp.float32)
    owner_rows = jnp.arange(blk_size)
    keep = jnp.where((owner_rows == blk_here)[:, None], 1.0 - near[None, :], 1.0)
    target_pieces = targets.reshape(6, blk_size, act_dev).transpose(1, 0, 2)

    def one_piece(items):
        target_piece, keep_piece = items
        weight = jnp.repeat(keep_piece, BLOCK)[None, :] * group_mass[None, :]
        return pair_sums(target_piece, group_src, weight)

    sums = lax.map(one_piece, (target_pieces, keep))
    partial_terms = sums.transpose(1, 0, 2).reshape(6, blk_size * act_dev)
    regular = reduce_halving(partial_terms, "blk")
    near_mass = (jnp.repeat(near, BLOCK) * group_mass)[None, :]
    irregular = pair_sums(own_set, group_src, near_mass)
    accel_now = regular[:3] + irregular[:3]
    jerk_now = regular[3:] + irregular[3:]
    step_time = jnp.take(elapsed, active_stars)
    start_accel = jnp.take(accel_old, active_stars, axis=1)
    start_jerk = jnp.take(jerk_old, active_stars, axis=1)
    change = start_accel - accel_now
    snap_term = -6.0 * change - step_time * (4.0 * start_jerk + 2.0 * jerk_now)
    crackle_term = 12.0 * change + 6.0 * step_time * (start_jerk + jerk_now)
    return (regular, irregular, jnp.concatenate([snap_term, crackle_term], axis=0))


def solution(mesh):
    in_specs = (
        P(None, ("blk", "grp")),
        P(None, ("blk", "grp")),
        P(None, ("blk", "grp")),
        P(None, ("blk", "grp")),
        P(("blk", "grp")),
        P(("blk", "grp")),
        P(("blk", "grp")),
        P(("blk", "grp"), None),
        P(("blk", "grp")),
    )
    out_specs = (P(None, ("blk", "grp")), P(None, ("blk", "grp")), P(None, ("blk", "grp")))
    return jax.shard_map(
        per_device, mesh=mesh, in_specs=in_specs, out_specs=out_specs, check_vma=False
    )
```

```python
import jax
import jax.numpy as jnp
from jax import lax
from jax.sharding import PartitionSpec as P


BLOCK = 128


soften_sq = 0.0001


def exchange(block, axis, bit):
    size = lax.axis_size(axis)
    return lax.ppermute(block, axis, [(i, i ^ bit) for i in range(size)])


def gather_doubling(block, axis):
    me = lax.axis_index(axis)
    bit = 1
    while bit < lax.axis_size(axis):
        got = exchange(block, axis, bit)
        upper = (me // bit) % 2 == 1
        block = jnp.where(
            upper, jnp.concatenate([got, block], 1), jnp.concatenate([block, got], 1)
        )
        bit *= 2
    return block


def reduce_halving(block, axis, bit):
    me = lax.axis_index(axis)
    while bit >= 1:
        width = block.shape[1] // 2
        low, high = block[:, :width], block[:, width:]
        upper = (me // bit) % 2 == 1
        keep = jnp.where(upper, high, low)
        send = jnp.where(upper, low, high)
        block = keep + exchange(send, axis, bit)
        bit //= 2
    return block


def gather_all_to_all(block, axis):
    size = lax.axis_size(axis)
    spread = jnp.broadcast_to(block[:, None, :], (block.shape[0], size, block.shape[1]))
    got = lax.all_to_all(spread, axis, 1, 1, tiled=True)
    return got.reshape(block.shape[0], size * block.shape[1])


def pair_sums(targets, sources, weight):
    gap_x = sources[0][None, :] - targets[0][:, None]
    gap_y = sources[1][None, :] - targets[1][:, None]
    gap_z = sources[2][None, :] - targets[2][:, None]
    rel_x = sources[3][None, :] - targets[3][:, None]
    rel_y = sources[4][None, :] - targets[4][:, None]
    rel_z = sources[5][None, :] - targets[5][:, None]
    dist_sq = gap_x * gap_x + gap_y * gap_y + gap_z * gap_z + soften_sq
    inverse = lax.rsqrt(dist_sq)
    scaled = weight * (inverse * inverse * inverse)
    radial = 3.0 * (gap_x * rel_x + gap_y * rel_y + gap_z * rel_z) / dist_sq
    term_list = [
        gap_x,
        gap_y,
        gap_z,
        rel_x - radial * gap_x,
        rel_y - radial * gap_y,
        rel_z - radial * gap_z,
    ]
    return jnp.stack([jnp.sum(scaled * term, axis=1) for term in term_list])


def per_device(
    position,
    velocity,
    accel_old,
    jerk_old,
    elapsed,
    masses,
    active_stars,
    neighbour_list,
    neighbour_count,
):
    moved_pos = position + elapsed * (
        velocity + elapsed * (0.5 * accel_old + elapsed * jerk_old / 6.0)
    )
    turned = velocity + elapsed * (accel_old + 0.5 * elapsed * jerk_old)
    sources = jnp.concatenate([moved_pos, turned], axis=0)
    own_set = jnp.take(sources, active_stars, axis=1)
    act_dev = active_stars.shape[0]
    block_data = jnp.concatenate([sources, masses[None, :]], axis=0)
    targets = gather_doubling(own_set, "blk")
    group = gather_all_to_all(block_data, "grp")
    group_src = group[:6]
    group_mass = group[6]
    blk_size = lax.axis_size("blk")
    blk_here = lax.axis_index("blk")
    block_total = group_src.shape[1] // BLOCK
    slot_total = neighbour_list.shape[1]
    own_live = jnp.arange(slot_total) < neighbour_count[0]
    near = jnp.any(
        own_live[:, None]
        & (neighbour_list[0][:, None] == jnp.arange(block_total)[None, :]),
        axis=0,
    ).astype(jnp.float32)
    half = blk_size // 2
    upper = (blk_here // half) % 2 == 1
    other_start = jnp.where(upper, 0, half)
    mine_start = half - other_start

    def half_sums(start):
        owners = start + jnp.arange(half)
        keep = jnp.where((owners == blk_here)[:, None], 1.0 - near[None, :], 1.0)
        pieces = lax.dynamic_slice_in_dim(targets, start * act_dev, half * act_dev, 1)
        pieces = pieces.reshape(6, half, act_dev).transpose(1, 0, 2)

        def one_piece(items):
            target_piece, keep_piece = items
            weight = jnp.repeat(keep_piece, BLOCK)[None, :] * group_mass[None, :]
            return pair_sums(target_piece, group_src, weight)

        sums = lax.map(one_piece, (pieces, keep))
        return sums.transpose(1, 0, 2).reshape(6, half * act_dev)

    send = half_sums(other_start)
    got = exchange(send, "blk", half)
    kept = half_sums(mine_start)
    regular = reduce_halving(kept + got, "blk", half // 2)
    near_mass = (jnp.repeat(near, BLOCK) * group_mass)[None, :]
    irregular = pair_sums(own_set, group_src, near_mass)
    accel_now = regular[:3] + irregular[:3]
    jerk_now = regular[3:] + irregular[3:]
    step_time = jnp.take(elapsed, active_stars)
    start_accel = jnp.take(accel_old, active_stars, axis=1)
    start_jerk = jnp.take(jerk_old, active_stars, axis=1)
    change = start_accel - accel_now
    snap_term = -6.0 * change - step_time * (4.0 * start_jerk + 2.0 * jerk_now)
    crackle_term = 12.0 * change + 6.0 * step_time * (start_jerk + jerk_now)
    return (regular, irregular, jnp.concatenate([snap_term, crackle_term], axis=0))


def solution(mesh):
    in_specs = (
        P(None, ("blk", "grp")),
        P(None, ("blk", "grp")),
        P(None, ("blk", "grp")),
        P(None, ("blk", "grp")),
        P(("blk", "grp")),
        P(("blk", "grp")),
        P(("blk", "grp")),
        P(("blk", "grp"), None),
        P(("blk", "grp")),
    )
    out_specs = (P(None, ("blk", "grp")), P(None, ("blk", "grp")), P(None, ("blk", "grp")))

    return jax.shard_map(
        per_device, mesh=mesh, in_specs=in_specs, out_specs=out_specs, check_vma=False
    )
```

```python
import jax
import jax.numpy as jnp
from jax import lax
from jax.sharding import PartitionSpec as P


BLOCK = 128


soften_sq = 0.0001


def exchange(block, axis, bit):
    size = lax.axis_size(axis)
    return lax.ppermute(block, axis, [(i, i ^ bit) for i in range(size)])


def gather_doubling(block, axis):
    me = lax.axis_index(axis)
    bit = 1
    while bit < lax.axis_size(axis):
        got = exchange(block, axis, bit)
        upper = (me // bit) % 2 == 1
        block = jnp.where(
            upper, jnp.concatenate([got, block], 1), jnp.concatenate([block, got], 1)
        )
        bit *= 2
    return block


def reduce_halving(block, axis, bit):
    me = lax.axis_index(axis)
    while bit >= 1:
        width = block.shape[1] // 2
        low, high = block[:, :width], block[:, width:]
        upper = (me // bit) % 2 == 1
        keep = jnp.where(upper, high, low)
        send = jnp.where(upper, low, high)
        block = keep + exchange(send, axis, bit)
        bit //= 2
    return block


def gather_all_to_all(block, axis):
    size = lax.axis_size(axis)
    spread = jnp.broadcast_to(block[:, None, :], (block.shape[0], size, block.shape[1]))
    got = lax.all_to_all(spread, axis, 1, 1, tiled=True)
    return got.reshape(block.shape[0], size * block.shape[1])


def pair_sums(targets, sources, weight):
    gap_x = sources[0][None, :] - targets[0][:, None]
    gap_y = sources[1][None, :] - targets[1][:, None]
    gap_z = sources[2][None, :] - targets[2][:, None]
    rel_x = sources[3][None, :] - targets[3][:, None]
    rel_y = sources[4][None, :] - targets[4][:, None]
    rel_z = sources[5][None, :] - targets[5][:, None]
    dist_sq = gap_x * gap_x + gap_y * gap_y + gap_z * gap_z + soften_sq
    inverse = lax.rsqrt(dist_sq)
    inverse_sq = inverse * inverse
    scaled = weight * (inverse_sq * inverse)
    radial = 3.0 * (gap_x * rel_x + gap_y * rel_y + gap_z * rel_z) * inverse_sq
    term_list = [
        gap_x,
        gap_y,
        gap_z,
        rel_x - radial * gap_x,
        rel_y - radial * gap_y,
        rel_z - radial * gap_z,
    ]
    return jnp.stack([jnp.sum(scaled * term, axis=1) for term in term_list])


def per_device(
    position,
    velocity,
    accel_old,
    jerk_old,
    elapsed,
    masses,
    active_stars,
    neighbour_list,
    neighbour_count,
):
    moved_pos = position + elapsed * (
        velocity + elapsed * (0.5 * accel_old + elapsed * jerk_old / 6.0)
    )
    turned = velocity + elapsed * (accel_old + 0.5 * elapsed * jerk_old)
    sources = jnp.concatenate([moved_pos, turned], axis=0)
    own_set = jnp.take(sources, active_stars, axis=1)
    act_dev = active_stars.shape[0]
    block_data = jnp.concatenate([sources, masses[None, :]], axis=0)
    targets = gather_doubling(own_set, "blk")
    group = gather_all_to_all(block_data, "grp")
    group_src = group[:6]
    group_mass = group[6]
    blk_size = lax.axis_size("blk")
    blk_here = lax.axis_index("blk")
    block_total = group_src.shape[1] // BLOCK
    slot_total = neighbour_list.shape[1]
    own_live = jnp.arange(slot_total) < neighbour_count[0]
    near = jnp.any(
        own_live[:, None]
        & (neighbour_list[0][:, None] == jnp.arange(block_total)[None, :]),
        axis=0,
    ).astype(jnp.float32)
    half = blk_size // 2
    upper = (blk_here // half) % 2 == 1
    other_start = jnp.where(upper, 0, half)
    mine_start = half - other_start

    def half_sums(start):
        owners = start + jnp.arange(half)
        keep = jnp.where((owners == blk_here)[:, None], 1.0 - near[None, :], 1.0)
        pieces = lax.dynamic_slice_in_dim(targets, start * act_dev, half * act_dev, 1)
        pieces = pieces.reshape(6, half, act_dev).transpose(1, 0, 2)

        def one_piece(items):
            target_piece, keep_piece = items
            weight = jnp.repeat(keep_piece, BLOCK)[None, :] * group_mass[None, :]
            return pair_sums(target_piece, group_src, weight)

        sums = lax.map(one_piece, (pieces, keep))
        return sums.transpose(1, 0, 2).reshape(6, half * act_dev)

    send = half_sums(other_start)
    got = exchange(send, "blk", half)
    kept = half_sums(mine_start)
    regular = reduce_halving(kept + got, "blk", half // 2)
    near_mass = (jnp.repeat(near, BLOCK) * group_mass)[None, :]
    irregular = pair_sums(own_set, group_src, near_mass)
    accel_now = regular[:3] + irregular[:3]
    jerk_now = regular[3:] + irregular[3:]
    step_time = jnp.take(elapsed, active_stars)
    start_accel = jnp.take(accel_old, active_stars, axis=1)
    start_jerk = jnp.take(jerk_old, active_stars, axis=1)
    change = start_accel - accel_now
    snap_term = -6.0 * change - step_time * (4.0 * start_jerk + 2.0 * jerk_now)
    crackle_term = 12.0 * change + 6.0 * step_time * (start_jerk + jerk_now)
    return (regular, irregular, jnp.concatenate([snap_term, crackle_term], axis=0))


def solution(mesh):
    in_specs = (
        P(None, ("blk", "grp")),
        P(None, ("blk", "grp")),
        P(None, ("blk", "grp")),
        P(None, ("blk", "grp")),
        P(("blk", "grp")),
        P(("blk", "grp")),
        P(("blk", "grp")),
        P(("blk", "grp"), None),
        P(("blk", "grp")),
    )
    out_specs = (P(None, ("blk", "grp")), P(None, ("blk", "grp")), P(None, ("blk", "grp")))

    return jax.shard_map(
        per_device, mesh=mesh, in_specs=in_specs, out_specs=out_specs, check_vma=False
    )
```

```python
import jax
import jax.numpy as jnp
from jax import lax
from jax.sharding import PartitionSpec as P


BLOCK = 128


soften_sq = 0.0001


def exchange(block, axis, bit):
    size = lax.axis_size(axis)
    return lax.ppermute(block, axis, [(i, i ^ bit) for i in range(size)])


def gather_doubling(block, axis):
    me = lax.axis_index(axis)
    bit = 1
    while bit < lax.axis_size(axis):
        got = exchange(block, axis, bit)
        upper = (me // bit) % 2 == 1
        block = jnp.where(
            upper, jnp.concatenate([got, block], 1), jnp.concatenate([block, got], 1)
        )
        bit *= 2
    return block


def gather_doubling_split(block, axis):
    me = lax.axis_index(axis)
    last = lax.axis_size(axis) // 2
    bit = 1
    while bit < last:
        got = exchange(block, axis, bit)
        upper = (me // bit) % 2 == 1
        block = jnp.where(
            upper, jnp.concatenate([got, block], 1), jnp.concatenate([block, got], 1)
        )
        bit *= 2
    got = exchange(block, axis, last)
    return block, got


def pair_terms(targets, sources):
    gap_x = sources[0][None, :] - targets[0][:, None]
    gap_y = sources[1][None, :] - targets[1][:, None]
    gap_z = sources[2][None, :] - targets[2][:, None]
    rel_x = sources[3][None, :] - targets[3][:, None]
    rel_y = sources[4][None, :] - targets[4][:, None]
    rel_z = sources[5][None, :] - targets[5][:, None]
    dist_sq = gap_x * gap_x + gap_y * gap_y + gap_z * gap_z + soften_sq
    inverse = lax.rsqrt(dist_sq)
    inv_cube = inverse * inverse * inverse
    radial = 3.0 * (gap_x * rel_x + gap_y * rel_y + gap_z * rel_z) / dist_sq
    term_list = [
        gap_x,
        gap_y,
        gap_z,
        rel_x - radial * gap_x,
        rel_y - radial * gap_y,
        rel_z - radial * gap_z,
    ]
    return inv_cube, term_list


def pair_sums(targets, sources, weight):
    inv_cube, term_list = pair_terms(targets, sources)
    scaled = weight * inv_cube
    return jnp.stack([jnp.sum(scaled * term, axis=1) for term in term_list])


def pair_sums_split(targets, sources, far_weight, near_weight):
    inv_cube, term_list = pair_terms(targets, sources)
    far_scaled = far_weight * inv_cube
    near_scaled = near_weight * inv_cube
    far = jnp.stack([jnp.sum(far_scaled * term, axis=1) for term in term_list])
    near = jnp.stack([jnp.sum(near_scaled * term, axis=1) for term in term_list])
    return far, near


def per_device(
    position,
    velocity,
    accel_old,
    jerk_old,
    elapsed,
    masses,
    active_stars,
    neighbour_list,
    neighbour_count,
):
    moved_pos = position + elapsed * (
        velocity + elapsed * (0.5 * accel_old + elapsed * jerk_old / 6.0)
    )
    turned = velocity + elapsed * (accel_old + 0.5 * elapsed * jerk_old)
    sources = jnp.concatenate([moved_pos, turned], axis=0)
    own_set = jnp.take(sources, active_stars, axis=1)
    act_dev = active_stars.shape[0]
    block_data = jnp.concatenate([sources, masses[None, :]], axis=0)
    targets = gather_doubling(own_set, "blk")
    near_half, far_half = gather_doubling_split(block_data, "grp")
    blk_size = lax.axis_size("blk")
    blk_here = lax.axis_index("blk")
    block_total = lax.axis_size("grp") * block_data.shape[1] // BLOCK
    slot_total = neighbour_list.shape[1]
    own_live = jnp.arange(slot_total) < neighbour_count[0]
    near = jnp.any(
        own_live[:, None]
        & (neighbour_list[0][:, None] == jnp.arange(block_total)[None, :]),
        axis=0,
    ).astype(jnp.float32)
    grp_here = lax.axis_index("grp")
    half_devices = lax.axis_size("grp") // 2
    blocks_half = near_half.shape[1] // BLOCK
    blocks_device = block_data.shape[1] // BLOCK
    near_start = (grp_here - grp_here % half_devices) * blocks_device
    far_device = grp_here ^ half_devices
    far_start = (far_device - far_device % half_devices) * blocks_device
    near_a = lax.dynamic_slice_in_dim(near, near_start, blocks_half)
    near_b = lax.dynamic_slice_in_dim(near, far_start, blocks_half)
    src_a, mass_a = near_half[:6], near_half[6]
    src_b, mass_b = far_half[:6], far_half[6]

    owners = jnp.arange(blk_size)
    keep = jnp.where((owners == blk_here)[:, None], 1.0 - near_a[None, :], 1.0)
    pieces = targets.reshape(6, blk_size, act_dev).transpose(1, 0, 2)

    def first_piece(items):
        target_piece, keep_piece = items
        piece_weight = jnp.repeat(keep_piece, BLOCK)[None, :] * mass_a[None, :]
        return pair_sums(target_piece, src_a, piece_weight)

    first = lax.map(first_piece, (pieces, keep))
    first = first.transpose(1, 0, 2).reshape(6, blk_size * act_dev)
    irregular_a = pair_sums(
        own_set, src_a, (jnp.repeat(near_a, BLOCK) * mass_a)[None, :]
    )

    weight = mass_b[None, :]

    def owner_sums(start, count):
        pieces = lax.dynamic_slice_in_dim(targets, start * act_dev, count * act_dev, 1)
        done = lax.dynamic_slice_in_dim(first, start * act_dev, count * act_dev, 1)
        if count == 1:
            return pair_sums(pieces, src_b, weight) + done
        pieces = pieces.reshape(6, count, act_dev).transpose(1, 0, 2)
        sums = lax.map(lambda piece: pair_sums(piece, src_b, weight), pieces)
        return sums.transpose(1, 0, 2).reshape(6, count * act_dev) + done

    def owner_cols(block, owner, span):
        return lax.dynamic_slice_in_dim(block, (owner % span) * act_dev, act_dev, 1)

    bit4, bit2 = blk_size // 2, blk_size // 4
    base4 = blk_here - blk_here % bit4
    start4 = blk_here - blk_here % (2 * bit4) + ((blk_here // bit4 + 1) % 2) * bit4
    sent4 = owner_sums(start4, bit4)
    got4 = exchange(sent4, "blk", bit4)
    start2 = base4 + ((blk_here // bit2 + 1) % 2) * bit2
    sent2 = owner_sums(start2, bit2) + lax.dynamic_slice_in_dim(
        got4, (start2 - base4) * act_dev, bit2 * act_dev, 1
    )
    got2 = exchange(sent2, "blk", bit2)
    partner = blk_here ^ 1
    sent1 = (
        owner_sums(partner, 1)
        + owner_cols(got4, partner, bit4)
        + owner_cols(got2, partner, bit2)
    )
    got1 = exchange(sent1, "blk", 1)
    near_rep = jnp.repeat(near_b, BLOCK)[None, :]
    own_far, irregular_b = pair_sums_split(
        own_set, src_b, weight * (1.0 - near_rep), weight * near_rep
    )
    regular = (
        own_far
        + owner_cols(first, blk_here, blk_size)
        + owner_cols(got4, blk_here, bit4)
        + owner_cols(got2, blk_here, bit2)
        + got1
    )
    irregular = irregular_a + irregular_b
    accel_now = regular[:3] + irregular[:3]
    jerk_now = regular[3:] + irregular[3:]
    step_time = jnp.take(elapsed, active_stars)
    start_accel = jnp.take(accel_old, active_stars, axis=1)
    start_jerk = jnp.take(jerk_old, active_stars, axis=1)
    change = start_accel - accel_now
    snap_term = -6.0 * change - step_time * (4.0 * start_jerk + 2.0 * jerk_now)
    crackle_term = 12.0 * change + 6.0 * step_time * (start_jerk + jerk_now)
    return (regular, irregular, jnp.concatenate([snap_term, crackle_term], axis=0))


def solution(mesh):
    in_specs = (
        P(None, ("blk", "grp")),
        P(None, ("blk", "grp")),
        P(None, ("blk", "grp")),
        P(None, ("blk", "grp")),
        P(("blk", "grp")),
        P(("blk", "grp")),
        P(("blk", "grp")),
        P(("blk", "grp"), None),
        P(("blk", "grp")),
    )
    out_specs = (P(None, ("blk", "grp")), P(None, ("blk", "grp")), P(None, ("blk", "grp")))

    return jax.shard_map(
        per_device, mesh=mesh, in_specs=in_specs, out_specs=out_specs, check_vma=False
    )
```

```python
import jax
import jax.numpy as jnp
from jax import lax
from jax.experimental import pallas as pl
from jax.experimental.pallas import tpu as pltpu
from jax.sharding import PartitionSpec as P
import functools


BLOCK = 128


soften_sq = 0.0001


def exchange(block, axis, bit):
    size = lax.axis_size(axis)
    return lax.ppermute(block, axis, [(i, i ^ bit) for i in range(size)])


def gather_doubling(block, axis):
    me = lax.axis_index(axis)
    bit = 1
    while bit < lax.axis_size(axis):
        got = exchange(block, axis, bit)
        upper = (me // bit) % 2 == 1
        block = jnp.where(
            upper, jnp.concatenate([got, block], 1), jnp.concatenate([block, got], 1)
        )
        bit *= 2
    return block


def gather_all_to_all(block, axis):
    size = lax.axis_size(axis)
    spread = jnp.broadcast_to(block[:, None, :], (block.shape[0], size, block.shape[1]))
    got = lax.all_to_all(spread, axis, 1, 1, tiled=True)
    return got.reshape(block.shape[0], size * block.shape[1])


LANES = 128
SUB = 8


def pair_kernel(tgt_ref, src_ref, out_ref, *, weights):
    rows = tgt_ref.shape[1]
    chunks = src_ref.shape[1] // LANES
    outs = 6 * weights

    def block_body(b, carry):
        r0 = pl.multiple_of(b * SUB, SUB)
        t = [tgt_ref[k, pl.ds(r0, SUB), :] for k in range(6)]

        def chunk_body(c, accs):
            c0 = pl.multiple_of(c * LANES, LANES)
            s = [
                jnp.broadcast_to(src_ref[pl.ds(k, 1), pl.ds(c0, LANES)], (SUB, LANES))
                for k in range(6 + weights)
            ]
            gap_x = s[0] - t[0]
            gap_y = s[1] - t[1]
            gap_z = s[2] - t[2]
            rel_x = s[3] - t[3]
            rel_y = s[4] - t[4]
            rel_z = s[5] - t[5]
            dist_sq = gap_x * gap_x + gap_y * gap_y + gap_z * gap_z + soften_sq
            inverse = lax.rsqrt(dist_sq)
            inv_cube = inverse * inverse * inverse
            radial = 3.0 * (gap_x * rel_x + gap_y * rel_y + gap_z * rel_z) / dist_sq
            terms = (
                gap_x,
                gap_y,
                gap_z,
                rel_x - radial * gap_x,
                rel_y - radial * gap_y,
                rel_z - radial * gap_z,
            )
            new = []
            for w in range(weights):
                scaled = s[6 + w] * inv_cube
                for i, term in enumerate(terms):
                    new.append(accs[6 * w + i] + scaled * term)
            return tuple(new)

        zeros = tuple(jnp.zeros((SUB, LANES), jnp.float32) for _ in range(outs))
        accs = lax.fori_loop(0, chunks, chunk_body, zeros, unroll=8)
        for i in range(outs):
            out_ref[pl.ds(r0, SUB), pl.ds(i, 1)] = jnp.sum(accs[i], axis=1, keepdims=True)
        return carry

    lax.fori_loop(0, rows // SUB, block_body, 0)


def kernel_sums(targets, src):
    rows = targets.shape[1]
    weights = src.shape[0] - 6
    sources = src[:6]
    tgt = jnp.broadcast_to(targets[:, :, None], (6, rows, LANES))
    pairs = rows * sources.shape[1]
    out = pl.pallas_call(
        functools.partial(pair_kernel, weights=weights),
        out_shape=jax.ShapeDtypeStruct((rows, LANES), jnp.float32),
        in_specs=[pl.BlockSpec(memory_space=pltpu.VMEM)] * 2,
        out_specs=pl.BlockSpec(memory_space=pltpu.VMEM),
        cost_estimate=pl.CostEstimate(
            flops=pairs * (30 + 12 * weights),
            transcendentals=pairs,
            bytes_accessed=4 * (tgt.size + src.size + rows * LANES),
        ),
    )(tgt, src)
    sums = out[:, : 6 * weights].T
    return [sums[6 * w : 6 * w + 6] for w in range(weights)]


def per_device(
    position,
    velocity,
    accel_old,
    jerk_old,
    elapsed,
    masses,
    active_stars,
    neighbour_list,
    neighbour_count,
):
    moved_pos = position + elapsed * (
        velocity + elapsed * (0.5 * accel_old + elapsed * jerk_old / 6.0)
    )
    turned = velocity + elapsed * (accel_old + 0.5 * elapsed * jerk_old)
    sources = jnp.concatenate([moved_pos, turned], axis=0)
    own_set = jnp.take(sources, active_stars, axis=1)
    act_dev = active_stars.shape[0]
    block_data = jnp.concatenate([sources, masses[None, :]], axis=0)
    targets = gather_doubling(own_set, "blk")
    group = gather_all_to_all(block_data, "grp")
    group_src = group[:6]
    group_mass = group[6]
    blk_size = lax.axis_size("blk")
    blk_here = lax.axis_index("blk")
    block_total = group_src.shape[1] // BLOCK
    slot_total = neighbour_list.shape[1]
    own_live = jnp.arange(slot_total) < neighbour_count[0]
    near = jnp.any(
        own_live[:, None]
        & (neighbour_list[0][:, None] == jnp.arange(block_total)[None, :]),
        axis=0,
    ).astype(jnp.float32)
    weight = group_mass[None, :]

    def owner_sums(start, count):
        pieces = lax.dynamic_slice_in_dim(targets, start * act_dev, count * act_dev, 1)
        return kernel_sums(pieces, group)[0]

    def owner_cols(block, owner, span):
        return lax.dynamic_slice_in_dim(block, (owner % span) * act_dev, act_dev, 1)

    bit4, bit2 = blk_size // 2, blk_size // 4
    base4 = blk_here - blk_here % bit4
    start4 = blk_here - blk_here % (2 * bit4) + ((blk_here // bit4 + 1) % 2) * bit4
    sent4 = owner_sums(start4, bit4)
    got4 = exchange(sent4, "blk", bit4)
    start2 = base4 + ((blk_here // bit2 + 1) % 2) * bit2
    sent2 = owner_sums(start2, bit2) + lax.dynamic_slice_in_dim(
        got4, (start2 - base4) * act_dev, bit2 * act_dev, 1
    )
    got2 = exchange(sent2, "blk", bit2)
    partner = blk_here ^ 1
    sent1 = (
        owner_sums(partner, 1)
        + owner_cols(got4, partner, bit4)
        + owner_cols(got2, partner, bit2)
    )
    got1 = exchange(sent1, "blk", 1)
    near_rep = jnp.repeat(near, BLOCK)[None, :]
    split_src = jnp.concatenate(
        [group_src, weight * (1.0 - near_rep), weight * near_rep], axis=0
    )
    own_far, irregular = kernel_sums(own_set, split_src)
    regular = (
        own_far
        + owner_cols(got4, blk_here, bit4)
        + owner_cols(got2, blk_here, bit2)
        + got1
    )
    accel_now = regular[:3] + irregular[:3]
    jerk_now = regular[3:] + irregular[3:]
    step_time = jnp.take(elapsed, active_stars)
    start_accel = jnp.take(accel_old, active_stars, axis=1)
    start_jerk = jnp.take(jerk_old, active_stars, axis=1)
    change = start_accel - accel_now
    snap_term = -6.0 * change - step_time * (4.0 * start_jerk + 2.0 * jerk_now)
    crackle_term = 12.0 * change + 6.0 * step_time * (start_jerk + jerk_now)
    return (regular, irregular, jnp.concatenate([snap_term, crackle_term], axis=0))


def solution(mesh):
    in_specs = (
        P(None, ("blk", "grp")),
        P(None, ("blk", "grp")),
        P(None, ("blk", "grp")),
        P(None, ("blk", "grp")),
        P(("blk", "grp")),
        P(("blk", "grp")),
        P(("blk", "grp")),
        P(("blk", "grp"), None),
        P(("blk", "grp")),
    )
    out_specs = (P(None, ("blk", "grp")), P(None, ("blk", "grp")), P(None, ("blk", "grp")))

    return jax.shard_map(
        per_device, mesh=mesh, in_specs=in_specs, out_specs=out_specs, check_vma=False
    )
```

```python
import jax
import jax.numpy as jnp
from jax import lax
from jax.sharding import PartitionSpec as P


BLOCK = 128


soften_sq = 0.0001


def exchange(block, axis, bit):
    size = lax.axis_size(axis)
    return lax.ppermute(block, axis, [(i, i ^ bit) for i in range(size)])


def gather_doubling(block, axis):
    me = lax.axis_index(axis)
    bit = 1
    while bit < lax.axis_size(axis):
        got = exchange(block, axis, bit)
        upper = (me // bit) % 2 == 1
        block = jnp.where(
            upper, jnp.concatenate([got, block], 1), jnp.concatenate([block, got], 1)
        )
        bit *= 2
    return block


def gather_all_to_all(block, axis):
    size = lax.axis_size(axis)
    spread = jnp.broadcast_to(block[:, None, :], (block.shape[0], size, block.shape[1]))
    got = lax.all_to_all(spread, axis, 1, 1, tiled=True)
    return got.reshape(block.shape[0], size * block.shape[1])


def pair_terms(targets, sources):
    gap_x = sources[0][None, :] - targets[0][:, None]
    gap_y = sources[1][None, :] - targets[1][:, None]
    gap_z = sources[2][None, :] - targets[2][:, None]
    rel_x = sources[3][None, :] - targets[3][:, None]
    rel_y = sources[4][None, :] - targets[4][:, None]
    rel_z = sources[5][None, :] - targets[5][:, None]
    dist_sq = gap_x * gap_x + gap_y * gap_y + gap_z * gap_z + soften_sq
    inverse = lax.rsqrt(dist_sq)
    inv_cube = inverse * inverse * inverse
    radial = 3.0 * (gap_x * rel_x + gap_y * rel_y + gap_z * rel_z) / dist_sq
    term_list = [
        gap_x,
        gap_y,
        gap_z,
        rel_x - radial * gap_x,
        rel_y - radial * gap_y,
        rel_z - radial * gap_z,
    ]
    return inv_cube, term_list


def pair_sums(targets, sources, weight):
    inv_cube, term_list = pair_terms(targets, sources)
    scaled = weight * inv_cube
    return jnp.stack([jnp.sum(scaled * term, axis=1) for term in term_list])


def pair_sums_split(targets, sources, far_weight, near_weight):
    inv_cube, term_list = pair_terms(targets, sources)
    far_scaled = far_weight * inv_cube
    near_scaled = near_weight * inv_cube
    far = jnp.stack([jnp.sum(far_scaled * term, axis=1) for term in term_list])
    near = jnp.stack([jnp.sum(near_scaled * term, axis=1) for term in term_list])
    return far, near


def per_device(
    position,
    velocity,
    accel_old,
    jerk_old,
    elapsed,
    masses,
    active_stars,
    neighbour_list,
    neighbour_count,
):
    def predict(pos, vel, acc, jerk, time):
        moved_pos = pos + time * (vel + time * (0.5 * acc + time * jerk / 6.0))
        turned = vel + time * (acc + 0.5 * time * jerk)
        return jnp.concatenate([moved_pos, turned], axis=0)

    raw = jnp.concatenate([position, velocity, accel_old, jerk_old, elapsed[None, :]], axis=0)
    raw_act = raw.at[:, active_stars].get(mode="promise_in_bounds")
    own_set = predict(raw_act[0:3], raw_act[3:6], raw_act[6:9], raw_act[9:12], raw_act[12])
    sources = predict(position, velocity, accel_old, jerk_old, elapsed)
    act_dev = active_stars.shape[0]
    block_data = jnp.concatenate([sources, masses[None, :]], axis=0)
    targets = gather_doubling(own_set, "blk")
    group = gather_all_to_all(block_data, "grp")
    group_src = group[:6]
    group_mass = group[6]
    blk_size = lax.axis_size("blk")
    blk_here = lax.axis_index("blk")
    block_total = group_src.shape[1] // BLOCK
    slot_total = neighbour_list.shape[1]
    own_live = jnp.arange(slot_total) < neighbour_count[0]
    near = jnp.any(
        own_live[:, None]
        & (neighbour_list[0][:, None] == jnp.arange(block_total)[None, :]),
        axis=0,
    ).astype(jnp.float32)
    weight = group_mass[None, :]

    def owner_sums(start, count):
        pieces = lax.dynamic_slice_in_dim(targets, start * act_dev, count * act_dev, 1)
        if count == 1:
            return pair_sums(pieces, group_src, weight)
        pieces = pieces.reshape(6, count, act_dev).transpose(1, 0, 2)
        sums = lax.map(lambda piece: pair_sums(piece, group_src, weight), pieces)
        return sums.transpose(1, 0, 2).reshape(6, count * act_dev)

    def owner_cols(block, owner, span):
        return lax.dynamic_slice_in_dim(block, (owner % span) * act_dev, act_dev, 1)

    bit4, bit2 = blk_size // 2, blk_size // 4
    base4 = blk_here - blk_here % bit4
    start4 = blk_here - blk_here % (2 * bit4) + ((blk_here // bit4 + 1) % 2) * bit4
    sent4 = owner_sums(start4, bit4)
    got4 = exchange(sent4, "blk", bit4)
    start2 = base4 + ((blk_here // bit2 + 1) % 2) * bit2
    sent2 = owner_sums(start2, bit2) + lax.dynamic_slice_in_dim(
        got4, (start2 - base4) * act_dev, bit2 * act_dev, 1
    )
    got2 = exchange(sent2, "blk", bit2)
    partner = blk_here ^ 1
    sent1 = (
        owner_sums(partner, 1)
        + owner_cols(got4, partner, bit4)
        + owner_cols(got2, partner, bit2)
    )
    got1 = exchange(sent1, "blk", 1)
    near_rep = jnp.repeat(near, BLOCK)[None, :]
    own_far, irregular = pair_sums_split(
        own_set, group_src, weight * (1.0 - near_rep), weight * near_rep
    )
    regular = (
        own_far
        + owner_cols(got4, blk_here, bit4)
        + owner_cols(got2, blk_here, bit2)
        + got1
    )
    accel_now = regular[:3] + irregular[:3]
    jerk_now = regular[3:] + irregular[3:]
    step_time = raw_act[12]
    start_accel = raw_act[6:9]
    start_jerk = raw_act[9:12]
    change = start_accel - accel_now
    snap_term = -6.0 * change - step_time * (4.0 * start_jerk + 2.0 * jerk_now)
    crackle_term = 12.0 * change + 6.0 * step_time * (start_jerk + jerk_now)
    return (regular, irregular, jnp.concatenate([snap_term, crackle_term], axis=0))


def solution(mesh):
    in_specs = (
        P(None, ("blk", "grp")),
        P(None, ("blk", "grp")),
        P(None, ("blk", "grp")),
        P(None, ("blk", "grp")),
        P(("blk", "grp")),
        P(("blk", "grp")),
        P(("blk", "grp")),
        P(("blk", "grp"), None),
        P(("blk", "grp")),
    )
    out_specs = (P(None, ("blk", "grp")), P(None, ("blk", "grp")), P(None, ("blk", "grp")))

    return jax.shard_map(
        per_device, mesh=mesh, in_specs=in_specs, out_specs=out_specs, check_vma=False
    )
```

```python
import jax
import jax.numpy as jnp
from jax import lax
from jax.sharding import PartitionSpec as P


BLOCK = 128


soften_sq = 0.0001


def exchange(block, axis, bit):
    size = lax.axis_size(axis)
    return lax.ppermute(block, axis, [(i, i ^ bit) for i in range(size)])


def gather_doubling(block, axis):
    me = lax.axis_index(axis)
    bit = 1
    while bit < lax.axis_size(axis):
        got = exchange(block, axis, bit)
        upper = (me // bit) % 2 == 1
        block = jnp.where(
            upper, jnp.concatenate([got, block], 1), jnp.concatenate([block, got], 1)
        )
        bit *= 2
    return block


def gather_all_to_all(block, axis):
    size = lax.axis_size(axis)
    spread = jnp.broadcast_to(block[:, None, :], (block.shape[0], size, block.shape[1]))
    got = lax.all_to_all(spread, axis, 1, 1, tiled=True)
    return got.reshape(block.shape[0], size * block.shape[1])


def pair_terms(targets, sources):
    gap_x = sources[0][None, :] - targets[0][:, None]
    gap_y = sources[1][None, :] - targets[1][:, None]
    gap_z = sources[2][None, :] - targets[2][:, None]
    rel_x = sources[3][None, :] - targets[3][:, None]
    rel_y = sources[4][None, :] - targets[4][:, None]
    rel_z = sources[5][None, :] - targets[5][:, None]
    dist_sq = gap_x * gap_x + gap_y * gap_y + gap_z * gap_z + soften_sq
    inverse = lax.rsqrt(dist_sq)
    inv_cube = inverse * inverse * inverse
    radial = 3.0 * (gap_x * rel_x + gap_y * rel_y + gap_z * rel_z) / dist_sq
    term_list = [
        gap_x,
        gap_y,
        gap_z,
        rel_x - radial * gap_x,
        rel_y - radial * gap_y,
        rel_z - radial * gap_z,
    ]
    return inv_cube, term_list


def pair_sums(targets, sources, weight):
    inv_cube, term_list = pair_terms(targets, sources)
    scaled = weight * inv_cube
    return jnp.stack([jnp.sum(scaled * term, axis=1) for term in term_list])


def pair_sums_split(targets, sources, far_weight, near_weight):
    inv_cube, term_list = pair_terms(targets, sources)
    far_scaled = far_weight * inv_cube
    near_scaled = near_weight * inv_cube
    far = jnp.stack([jnp.sum(far_scaled * term, axis=1) for term in term_list])
    near = jnp.stack([jnp.sum(near_scaled * term, axis=1) for term in term_list])
    return far, near


def per_device(
    position,
    velocity,
    accel_old,
    jerk_old,
    elapsed,
    masses,
    active_stars,
    neighbour_list,
    neighbour_count,
):
    moved_pos = position + elapsed * (
        velocity + elapsed * (0.5 * accel_old + elapsed * jerk_old / 6.0)
    )
    turned = velocity + elapsed * (accel_old + 0.5 * elapsed * jerk_old)
    sources = jnp.concatenate([moved_pos, turned], axis=0)
    own_set = jnp.take(sources, active_stars, axis=1)
    act_dev = active_stars.shape[0]
    block_data = jnp.concatenate([sources, masses[None, :]], axis=0)
    targets = gather_doubling(own_set, "blk")
    group = gather_all_to_all(block_data, "grp")
    group_src = group[:6]
    group_mass = group[6]
    blk_size = lax.axis_size("blk")
    blk_here = lax.axis_index("blk")
    block_total = group_src.shape[1] // BLOCK
    slot_total = neighbour_list.shape[1]
    own_live = jnp.arange(slot_total) < neighbour_count[0]
    near = jnp.any(
        own_live[:, None]
        & (neighbour_list[0][:, None] == jnp.arange(block_total)[None, :]),
        axis=0,
    ).astype(jnp.float32)
    weight = group_mass[None, :]

    def owner_sums(start, count):
        pieces = lax.dynamic_slice_in_dim(targets, start * act_dev, count * act_dev, 1)
        return pair_sums(pieces, group_src, weight)

    def owner_cols(block, owner, span):
        return lax.dynamic_slice_in_dim(block, (owner % span) * act_dev, act_dev, 1)

    bit4, bit2 = blk_size // 2, blk_size // 4
    base4 = blk_here - blk_here % bit4
    start4 = blk_here - blk_here % (2 * bit4) + ((blk_here // bit4 + 1) % 2) * bit4
    sent4 = owner_sums(start4, bit4)
    got4 = exchange(sent4, "blk", bit4)
    start2 = base4 + ((blk_here // bit2 + 1) % 2) * bit2
    sent2 = owner_sums(start2, bit2) + lax.dynamic_slice_in_dim(
        got4, (start2 - base4) * act_dev, bit2 * act_dev, 1
    )
    got2 = exchange(sent2, "blk", bit2)
    partner = blk_here ^ 1
    sent1 = (
        owner_sums(partner, 1)
        + owner_cols(got4, partner, bit4)
        + owner_cols(got2, partner, bit2)
    )
    got1 = exchange(sent1, "blk", 1)
    near_rep = jnp.repeat(near, BLOCK)[None, :]
    own_far, irregular = pair_sums_split(
        own_set, group_src, weight * (1.0 - near_rep), weight * near_rep
    )
    regular = (
        own_far
        + owner_cols(got4, blk_here, bit4)
        + owner_cols(got2, blk_here, bit2)
        + got1
    )
    accel_now = regular[:3] + irregular[:3]
    jerk_now = regular[3:] + irregular[3:]
    step_time = jnp.take(elapsed, active_stars)
    start_accel = jnp.take(accel_old, active_stars, axis=1)
    start_jerk = jnp.take(jerk_old, active_stars, axis=1)
    change = start_accel - accel_now
    snap_term = -6.0 * change - step_time * (4.0 * start_jerk + 2.0 * jerk_now)
    crackle_term = 12.0 * change + 6.0 * step_time * (start_jerk + jerk_now)
    return (regular, irregular, jnp.concatenate([snap_term, crackle_term], axis=0))


def solution(mesh):
    in_specs = (
        P(None, ("blk", "grp")),
        P(None, ("blk", "grp")),
        P(None, ("blk", "grp")),
        P(None, ("blk", "grp")),
        P(("blk", "grp")),
        P(("blk", "grp")),
        P(("blk", "grp")),
        P(("blk", "grp"), None),
        P(("blk", "grp")),
    )
    out_specs = (P(None, ("blk", "grp")), P(None, ("blk", "grp")), P(None, ("blk", "grp")))

    return jax.shard_map(
        per_device, mesh=mesh, in_specs=in_specs, out_specs=out_specs, check_vma=False
    )
```

```python
import jax
import jax.numpy as jnp
from jax import lax
from jax.sharding import PartitionSpec as P


BLOCK = 128


soften_sq = 0.0001


def exchange(block, axis, bit):
    size = lax.axis_size(axis)
    return lax.ppermute(block, axis, [(i, i ^ bit) for i in range(size)])


def gather_doubling(block, axis):
    me = lax.axis_index(axis)
    bit = 1
    while bit < lax.axis_size(axis):
        got = exchange(block, axis, bit)
        upper = (me // bit) % 2 == 1
        block = jnp.where(
            upper, jnp.concatenate([got, block], 1), jnp.concatenate([block, got], 1)
        )
        bit *= 2
    return block


def gather_all_to_all(block, axis):
    size = lax.axis_size(axis)
    spread = jnp.broadcast_to(block[:, None, :], (block.shape[0], size, block.shape[1]))
    got = lax.all_to_all(spread, axis, 1, 1, tiled=True)
    return got.reshape(block.shape[0], size * block.shape[1])


def pair_terms(targets, sources):
    gap_x = sources[0][None, :] - targets[0][:, None]
    gap_y = sources[1][None, :] - targets[1][:, None]
    gap_z = sources[2][None, :] - targets[2][:, None]
    rel_x = sources[3][None, :] - targets[3][:, None]
    rel_y = sources[4][None, :] - targets[4][:, None]
    rel_z = sources[5][None, :] - targets[5][:, None]
    dist_sq = gap_x * gap_x + gap_y * gap_y + gap_z * gap_z + soften_sq
    inverse = lax.rsqrt(dist_sq)
    inv_cube = inverse * inverse * inverse
    radial = 3.0 * (gap_x * rel_x + gap_y * rel_y + gap_z * rel_z) / dist_sq
    term_list = [
        gap_x,
        gap_y,
        gap_z,
        rel_x - radial * gap_x,
        rel_y - radial * gap_y,
        rel_z - radial * gap_z,
    ]
    return inv_cube, term_list


def pair_sums(targets, sources, weight):
    inv_cube, term_list = pair_terms(targets, sources)
    scaled = weight * inv_cube
    return jnp.stack([jnp.sum(scaled * term, axis=1) for term in term_list])


def pair_sums_split(targets, sources, far_weight, near_weight):
    inv_cube, term_list = pair_terms(targets, sources)
    far_scaled = far_weight * inv_cube
    near_scaled = near_weight * inv_cube
    far = jnp.stack([jnp.sum(far_scaled * term, axis=1) for term in term_list])
    near = jnp.stack([jnp.sum(near_scaled * term, axis=1) for term in term_list])
    return far, near


def per_device(
    position,
    velocity,
    accel_old,
    jerk_old,
    elapsed,
    masses,
    active_stars,
    neighbour_list,
    neighbour_count,
):
    moved_pos = position + elapsed * (
        velocity + elapsed * (0.5 * accel_old + elapsed * jerk_old / 6.0)
    )
    turned = velocity + elapsed * (accel_old + 0.5 * elapsed * jerk_old)
    sources = jnp.concatenate([moved_pos, turned], axis=0)
    picks = (active_stars[None, :] == jnp.arange(sources.shape[1])[:, None]).astype(jnp.float32)
    own_set = jnp.dot(sources, picks, precision=lax.Precision.HIGHEST)
    act_dev = active_stars.shape[0]
    block_data = jnp.concatenate([sources, masses[None, :]], axis=0)
    targets = gather_doubling(own_set, "blk")
    group = gather_all_to_all(block_data, "grp")
    group_src = group[:6]
    group_mass = group[6]
    blk_size = lax.axis_size("blk")
    blk_here = lax.axis_index("blk")
    block_total = group_src.shape[1] // BLOCK
    slot_total = neighbour_list.shape[1]
    own_live = jnp.arange(slot_total) < neighbour_count[0]
    near = jnp.any(
        own_live[:, None]
        & (neighbour_list[0][:, None] == jnp.arange(block_total)[None, :]),
        axis=0,
    ).astype(jnp.float32)
    weight = group_mass[None, :]

    def owner_sums(start, count):
        pieces = lax.dynamic_slice_in_dim(targets, start * act_dev, count * act_dev, 1)
        return pair_sums(pieces, group_src, weight)

    def owner_cols(block, owner, span):
        return lax.dynamic_slice_in_dim(block, (owner % span) * act_dev, act_dev, 1)

    bit4, bit2 = blk_size // 2, blk_size // 4
    base4 = blk_here - blk_here % bit4
    start4 = blk_here - blk_here % (2 * bit4) + ((blk_here // bit4 + 1) % 2) * bit4
    sent4 = owner_sums(start4, bit4)
    got4 = exchange(sent4, "blk", bit4)
    start2 = base4 + ((blk_here // bit2 + 1) % 2) * bit2
    sent2 = owner_sums(start2, bit2) + lax.dynamic_slice_in_dim(
        got4, (start2 - base4) * act_dev, bit2 * act_dev, 1
    )
    got2 = exchange(sent2, "blk", bit2)
    partner = blk_here ^ 1
    sent1 = (
        owner_sums(partner, 1)
        + owner_cols(got4, partner, bit4)
        + owner_cols(got2, partner, bit2)
    )
    got1 = exchange(sent1, "blk", 1)
    near_rep = jnp.repeat(near, BLOCK)[None, :]
    own_far, irregular = pair_sums_split(
        own_set, group_src, weight * (1.0 - near_rep), weight * near_rep
    )
    regular = (
        own_far
        + owner_cols(got4, blk_here, bit4)
        + owner_cols(got2, blk_here, bit2)
        + got1
    )
    accel_now = regular[:3] + irregular[:3]
    jerk_now = regular[3:] + irregular[3:]
    step_time = elapsed.at[active_stars].get(mode="promise_in_bounds")
    start_accel = accel_old.at[:, active_stars].get(mode="promise_in_bounds")
    start_jerk = jerk_old.at[:, active_stars].get(mode="promise_in_bounds")
    change = start_accel - accel_now
    snap_term = -6.0 * change - step_time * (4.0 * start_jerk + 2.0 * jerk_now)
    crackle_term = 12.0 * change + 6.0 * step_time * (start_jerk + jerk_now)
    return (regular, irregular, jnp.concatenate([snap_term, crackle_term], axis=0))


def solution(mesh):
    in_specs = (
        P(None, ("blk", "grp")),
        P(None, ("blk", "grp")),
        P(None, ("blk", "grp")),
        P(None, ("blk", "grp")),
        P(("blk", "grp")),
        P(("blk", "grp")),
        P(("blk", "grp")),
        P(("blk", "grp"), None),
        P(("blk", "grp")),
    )
    out_specs = (P(None, ("blk", "grp")), P(None, ("blk", "grp")), P(None, ("blk", "grp")))

    return jax.shard_map(
        per_device, mesh=mesh, in_specs=in_specs, out_specs=out_specs, check_vma=False
    )
```

```python
import jax
import jax.numpy as jnp
from jax import lax
from jax.sharding import PartitionSpec as P


BLOCK = 128


soften_sq = 0.0001


def exchange(block, axis, bit):
    size = lax.axis_size(axis)
    return lax.ppermute(block, axis, [(i, i ^ bit) for i in range(size)])


def gather_doubling(block, axis):
    me = lax.axis_index(axis)
    bit = 1
    while bit < lax.axis_size(axis):
        got = exchange(block, axis, bit)
        upper = (me // bit) % 2 == 1
        block = jnp.where(
            upper, jnp.concatenate([got, block], 1), jnp.concatenate([block, got], 1)
        )
        bit *= 2
    return block


def gather_all_to_all(block, axis):
    size = lax.axis_size(axis)
    spread = jnp.broadcast_to(block[:, None, :], (block.shape[0], size, block.shape[1]))
    got = lax.all_to_all(spread, axis, 1, 1, tiled=True)
    return got.reshape(block.shape[0], size * block.shape[1])


def pair_terms(targets, sources):
    gap_x = sources[0][None, :] - targets[0][:, None]
    gap_y = sources[1][None, :] - targets[1][:, None]
    gap_z = sources[2][None, :] - targets[2][:, None]
    rel_x = sources[3][None, :] - targets[3][:, None]
    rel_y = sources[4][None, :] - targets[4][:, None]
    rel_z = sources[5][None, :] - targets[5][:, None]
    dist_sq = gap_x * gap_x + gap_y * gap_y + gap_z * gap_z + soften_sq
    inverse = lax.rsqrt(dist_sq)
    inv_cube = inverse * inverse * inverse
    radial = 3.0 * (gap_x * rel_x + gap_y * rel_y + gap_z * rel_z) / dist_sq
    term_list = [
        gap_x,
        gap_y,
        gap_z,
        rel_x - radial * gap_x,
        rel_y - radial * gap_y,
        rel_z - radial * gap_z,
    ]
    return inv_cube, term_list


def two_stage_sums(scaled, term_list, groups=2):
    rows, width = scaled.shape
    partial = jnp.stack(
        [
            jnp.sum((scaled * term).reshape(rows, groups, width // groups), axis=2)
            for term in term_list
        ]
    )
    return jnp.sum(lax.optimization_barrier(partial), axis=2)


def pair_sums(targets, sources, weight):
    inv_cube, term_list = pair_terms(targets, sources)
    scaled = weight * inv_cube
    return two_stage_sums(scaled, term_list)


def pair_sums_split(targets, sources, far_weight, near_weight):
    inv_cube, term_list = pair_terms(targets, sources)
    far = two_stage_sums(far_weight * inv_cube, term_list)
    near = two_stage_sums(near_weight * inv_cube, term_list)
    return far, near


def per_device(
    position,
    velocity,
    accel_old,
    jerk_old,
    elapsed,
    masses,
    active_stars,
    neighbour_list,
    neighbour_count,
):
    moved_pos = position + elapsed * (
        velocity + elapsed * (0.5 * accel_old + elapsed * jerk_old / 6.0)
    )
    turned = velocity + elapsed * (accel_old + 0.5 * elapsed * jerk_old)
    sources = jnp.concatenate([moved_pos, turned], axis=0)
    picks = (active_stars[None, :] == jnp.arange(sources.shape[1])[:, None]).astype(jnp.float32)
    own_set = jnp.dot(sources, picks, precision=lax.Precision.HIGHEST)
    act_dev = active_stars.shape[0]
    block_data = jnp.concatenate([sources, masses[None, :]], axis=0)
    targets = gather_doubling(own_set, "blk")
    group = gather_all_to_all(block_data, "grp")
    group_src = group[:6]
    group_mass = group[6]
    blk_size = lax.axis_size("blk")
    blk_here = lax.axis_index("blk")
    block_total = group_src.shape[1] // BLOCK
    slot_total = neighbour_list.shape[1]
    own_live = jnp.arange(slot_total) < neighbour_count[0]
    near = jnp.any(
        own_live[:, None]
        & (neighbour_list[0][:, None] == jnp.arange(block_total)[None, :]),
        axis=0,
    ).astype(jnp.float32)
    weight = group_mass[None, :]

    def owner_sums(start, count):
        pieces = lax.dynamic_slice_in_dim(targets, start * act_dev, count * act_dev, 1)
        return pair_sums(pieces, group_src, weight)

    def owner_cols(block, owner, span):
        return lax.dynamic_slice_in_dim(block, (owner % span) * act_dev, act_dev, 1)

    bit4, bit2 = blk_size // 2, blk_size // 4
    base4 = blk_here - blk_here % bit4
    start4 = blk_here - blk_here % (2 * bit4) + ((blk_here // bit4 + 1) % 2) * bit4
    sent4 = owner_sums(start4, bit4)
    got4 = exchange(sent4, "blk", bit4)
    start2 = base4 + ((blk_here // bit2 + 1) % 2) * bit2
    sent2 = owner_sums(start2, bit2) + lax.dynamic_slice_in_dim(
        got4, (start2 - base4) * act_dev, bit2 * act_dev, 1
    )
    got2 = exchange(sent2, "blk", bit2)
    partner = blk_here ^ 1
    sent1 = (
        owner_sums(partner, 1)
        + owner_cols(got4, partner, bit4)
        + owner_cols(got2, partner, bit2)
    )
    got1 = exchange(sent1, "blk", 1)
    near_rep = jnp.repeat(near, BLOCK)[None, :]
    own_far, irregular = pair_sums_split(
        own_set, group_src, weight * (1.0 - near_rep), weight * near_rep
    )
    regular = (
        own_far
        + owner_cols(got4, blk_here, bit4)
        + owner_cols(got2, blk_here, bit2)
        + got1
    )
    accel_now = regular[:3] + irregular[:3]
    jerk_now = regular[3:] + irregular[3:]
    step_time = elapsed.at[active_stars].get(mode="promise_in_bounds")
    start_accel = accel_old.at[:, active_stars].get(mode="promise_in_bounds")
    start_jerk = jerk_old.at[:, active_stars].get(mode="promise_in_bounds")
    change = start_accel - accel_now
    snap_term = -6.0 * change - step_time * (4.0 * start_jerk + 2.0 * jerk_now)
    crackle_term = 12.0 * change + 6.0 * step_time * (start_jerk + jerk_now)
    return (regular, irregular, jnp.concatenate([snap_term, crackle_term], axis=0))


def solution(mesh):
    in_specs = (
        P(None, ("blk", "grp")),
        P(None, ("blk", "grp")),
        P(None, ("blk", "grp")),
        P(None, ("blk", "grp")),
        P(("blk", "grp")),
        P(("blk", "grp")),
        P(("blk", "grp")),
        P(("blk", "grp"), None),
        P(("blk", "grp")),
    )
    out_specs = (P(None, ("blk", "grp")), P(None, ("blk", "grp")), P(None, ("blk", "grp")))

    return jax.shard_map(
        per_device, mesh=mesh, in_specs=in_specs, out_specs=out_specs, check_vma=False
    )
```

```python
import jax
import jax.numpy as jnp
from jax import lax
from jax.sharding import PartitionSpec as P


BLOCK = 128


soften_sq = 0.0001


def exchange(block, axis, bit):
    size = lax.axis_size(axis)
    return lax.ppermute(block, axis, [(i, i ^ bit) for i in range(size)])


def gather_doubling(block, axis, first=1):
    me = lax.axis_index(axis)
    bit = first
    while bit < lax.axis_size(axis):
        got = exchange(block, axis, bit)
        upper = (me // bit) % 2 == 1
        block = jnp.where(
            upper, jnp.concatenate([got, block], 1), jnp.concatenate([block, got], 1)
        )
        bit *= 2
    return block


def gather_all_to_all(block, axis):
    size = lax.axis_size(axis)
    spread = jnp.broadcast_to(block[:, None, :], (block.shape[0], size, block.shape[1]))
    got = lax.all_to_all(spread, axis, 1, 1, tiled=True)
    return got.reshape(block.shape[0], size * block.shape[1])


def pair_terms(targets, sources):
    gap_x = sources[0][None, :] - targets[0][:, None]
    gap_y = sources[1][None, :] - targets[1][:, None]
    gap_z = sources[2][None, :] - targets[2][:, None]
    rel_x = sources[3][None, :] - targets[3][:, None]
    rel_y = sources[4][None, :] - targets[4][:, None]
    rel_z = sources[5][None, :] - targets[5][:, None]
    dist_sq = gap_x * gap_x + gap_y * gap_y + gap_z * gap_z + soften_sq
    inverse = lax.rsqrt(dist_sq)
    inv_cube = inverse * inverse * inverse
    radial = 3.0 * (gap_x * rel_x + gap_y * rel_y + gap_z * rel_z) / dist_sq
    term_list = [
        gap_x,
        gap_y,
        gap_z,
        rel_x - radial * gap_x,
        rel_y - radial * gap_y,
        rel_z - radial * gap_z,
    ]
    return inv_cube, term_list


def pair_sums(targets, sources, weight):
    inv_cube, term_list = pair_terms(targets, sources)
    scaled = weight * inv_cube
    return jnp.stack([jnp.sum(scaled * term, axis=1) for term in term_list])


def pair_sums_split(targets, sources, far_weight, near_weight):
    inv_cube, term_list = pair_terms(targets, sources)
    far_scaled = far_weight * inv_cube
    near_scaled = near_weight * inv_cube
    far = jnp.stack([jnp.sum(far_scaled * term, axis=1) for term in term_list])
    near = jnp.stack([jnp.sum(near_scaled * term, axis=1) for term in term_list])
    return far, near


def per_device(
    position,
    velocity,
    accel_old,
    jerk_old,
    elapsed,
    masses,
    active_stars,
    neighbour_list,
    neighbour_count,
):
    moved_pos = position + elapsed * (
        velocity + elapsed * (0.5 * accel_old + elapsed * jerk_old / 6.0)
    )
    turned = velocity + elapsed * (accel_old + 0.5 * (elapsed * jerk_old))
    sources = jnp.concatenate([moved_pos, turned], axis=0)
    res_dev = sources.shape[1]
    act_dev = active_stars.shape[0]

    def select(block, index):
        picks = (index[None, :] == jnp.arange(res_dev)[:, None]).astype(jnp.float32)
        return jnp.dot(block, picks, precision=lax.Precision.HIGHEST)

    own_set = select(sources, active_stars)
    block_data = jnp.concatenate([sources, masses[None, :]], axis=0)
    index_row = jnp.pad(active_stars.astype(jnp.float32), (0, res_dev - act_dev))
    got = exchange(jnp.concatenate([sources, index_row[None, :]], 0), "blk", 1)
    other_set = select(got[:6], got[6, :act_dev].astype(jnp.int32))
    upper = lax.axis_index("blk") % 2 == 1
    pair = jnp.where(
        upper,
        jnp.concatenate([other_set, own_set], 1),
        jnp.concatenate([own_set, other_set], 1),
    )
    targets = gather_doubling(pair, "blk", first=2)
    group = gather_all_to_all(block_data, "grp")
    group_src = group[:6]
    group_mass = group[6]
    blk_size = lax.axis_size("blk")
    blk_here = lax.axis_index("blk")
    block_total = group_src.shape[1] // BLOCK
    slot_total = neighbour_list.shape[1]
    own_live = jnp.arange(slot_total) < neighbour_count[0]
    near = jnp.any(
        own_live[:, None]
        & (neighbour_list[0][:, None] == jnp.arange(block_total)[None, :]),
        axis=0,
    ).astype(jnp.float32)
    weight = group_mass[None, :]

    def owner_sums(start, count):
        pieces = lax.dynamic_slice_in_dim(targets, start * act_dev, count * act_dev, 1)
        return pair_sums(pieces, group_src, weight)

    def owner_cols(block, owner, span):
        return lax.dynamic_slice_in_dim(block, (owner % span) * act_dev, act_dev, 1)

    bit4, bit2 = blk_size // 2, blk_size // 4
    base4 = blk_here - blk_here % bit4
    start4 = blk_here - blk_here % (2 * bit4) + ((blk_here // bit4 + 1) % 2) * bit4
    sent4 = owner_sums(start4, bit4)
    got4 = exchange(sent4, "blk", bit4)
    start2 = base4 + ((blk_here // bit2 + 1) % 2) * bit2
    sent2 = owner_sums(start2, bit2) + lax.dynamic_slice_in_dim(
        got4, (start2 - base4) * act_dev, bit2 * act_dev, 1
    )
    got2 = exchange(sent2, "blk", bit2)
    partner = blk_here ^ 1
    sent1 = (
        owner_sums(partner, 1)
        + owner_cols(got4, partner, bit4)
        + owner_cols(got2, partner, bit2)
    )
    got1 = exchange(sent1, "blk", 1)
    near_rep = jnp.repeat(near, BLOCK)[None, :]
    own_far, irregular = pair_sums_split(
        own_set, group_src, weight * (1.0 - near_rep), weight * near_rep
    )
    regular = (
        own_far
        + owner_cols(got4, blk_here, bit4)
        + owner_cols(got2, blk_here, bit2)
        + got1
    )
    accel_now = regular[:3] + irregular[:3]
    jerk_now = regular[3:] + irregular[3:]
    step_time = elapsed.at[active_stars].get(mode="promise_in_bounds")
    start_accel = accel_old.at[:, active_stars].get(mode="promise_in_bounds")
    start_jerk = jerk_old.at[:, active_stars].get(mode="promise_in_bounds")
    change = start_accel - accel_now
    snap_term = -6.0 * change - step_time * (4.0 * start_jerk + 2.0 * jerk_now)
    crackle_term = 12.0 * change + 6.0 * step_time * (start_jerk + jerk_now)
    return (regular, irregular, jnp.concatenate([snap_term, crackle_term], axis=0))


def solution(mesh):
    in_specs = (
        P(None, ("blk", "grp")),
        P(None, ("blk", "grp")),
        P(None, ("blk", "grp")),
        P(None, ("blk", "grp")),
        P(("blk", "grp")),
        P(("blk", "grp")),
        P(("blk", "grp")),
        P(("blk", "grp"), None),
        P(("blk", "grp")),
    )
    out_specs = (P(None, ("blk", "grp")), P(None, ("blk", "grp")), P(None, ("blk", "grp")))

    return jax.shard_map(
        per_device, mesh=mesh, in_specs=in_specs, out_specs=out_specs, check_vma=False
    )
```
